32 devices in a mesh: narrow: 4 (over y, core), wide: 8 (over z, x).
Axes of the slice: x: 2, y: 2, z: 4, core: 2. Of those that a mesh axis runs over, the one named last changes fastest.
Arguments:
- hidden_in: bfloat16 [256, 16384], P('narrow', 'wide'), may hold values from -6 to 6
- w_query: bfloat16 [16384, 8, 2048], P('wide', 'narrow'), may hold values from -0.046875 to 0.046875
- w_keyval: bfloat16 [16384, 8, 256], P('wide', 'narrow'), may hold values from -0.046875 to 0.046875
- w_out: bfloat16 [16384, 16384], P('narrow', 'wide'), may hold values from -0.125 to 0.125
- key_cache: bfloat16 [256, 8, 1024, 128], P('wide', 'narrow'), may hold values from -1300 to 1300
- value_cache: bfloat16 [256, 8, 1024, 128], P('wide', 'narrow'), may hold values from -6 to 6
- lengths: int32 [256], P('wide'), may hold values from 2 to 1024, as said below
Outputs:
- hidden_out: bfloat16 [256, 16384], P('narrow', 'wide')
The draws below stay inside these ranges and needn't reach their ends.
Inputs may be any that keep to these rules, and one draw needn't show every extreme that they name: `lengths`: each row holds at least 2 cached tokens; some row holds exactly 1024.
All inputs are finite; a program needn't handle non-finite values.
Results may differ from the reference program's by a relative error of at most 0.019.
The reference program's roundings to bfloat16 on the way count: a program that leaves them out, or rounds other values in their place, can miss the bound.
Values may be sent and summed in bfloat16 or wider, within the bound.
No kernel may reach another device: no remote copies, remote signals or barrier semaphores. Data moves between devices by JAX's collectives and lax.ppermute only.
A program may use at most 192 MiB of HBM per device.

```python
import jax
import jax.numpy as jnp
from jax import lax

D = 16384
HEADS = 128
KV_HEADS = 8
HEAD_DIM = 128
CACHE = 1024
STEPS = 2
GROUP = 16
ROWS = 256


def draw_lengths(key, part):
    first, second = jax.random.split(key)
    values = jax.random.randint(first, (ROWS,), 2, CACHE + 1)
    spot = jax.random.randint(second, (), 0, ROWS)
    return values.at[spot].set(CACHE).astype(jnp.int32)


def draw_key_cache(key, part):
    first = jax.random.fold_in(key, 0)
    base = jnp.clip(jax.random.normal(first, (ROWS, KV_HEADS, CACHE, HEAD_DIM), jnp.float32), -4.0, 4.0)
    return base.astype(jnp.bfloat16)


def block_scale(own_key, dims, shards, smallest, top_value):
    loudness, own = 1.0, jax.random.fold_in(own_key, 6)
    for axis_at, parts in shards:
        steps = jnp.exp(jax.random.uniform(jax.random.fold_in(own, axis_at), (parts,), jnp.float32, smallest / len(shards), top_value / len(shards)))
        loudness = loudness * jnp.repeat(steps, dims[axis_at] // parts).reshape([-1 if axis == axis_at else 1 for axis in range(len(dims))])
    return loudness


def scatter_about(stream_key, dims, deviation, limit, cuts=(), kind=jnp.bfloat16):
    entries = deviation * jax.random.normal(stream_key, dims, jnp.float32)
    if cuts:
        entries = entries * block_scale(stream_key, dims, cuts, -0.22, 0.18)
    return jnp.clip(entries, -limit, limit).astype(kind)


def setup_inputs(seed: int = 0) -> dict:
    seeds = jax.random.split(jax.random.key(seed), 8)
    return {
        "hidden_in": scatter_about(seeds[0], (ROWS, D), 1.0, 6.0, ((0, 4), (1, 8))),
        "w_query": scatter_about(seeds[1], (D, KV_HEADS, GROUP * HEAD_DIM), D ** -0.5, 0.046875, ((0, 8), (1, 4))),
        "w_keyval": scatter_about(seeds[2], (D, KV_HEADS, 2 * HEAD_DIM), D ** -0.5, 0.046875, ((0, 8), (1, 4))),
        "w_out": scatter_about(seeds[3], (HEADS * HEAD_DIM, D), (GROUP * HEAD_DIM) ** -0.5, 0.125, ((0, 4), (1, 8))),
        "key_cache": draw_key_cache(jax.random.fold_in(seeds[7], 71), 0),
        "value_cache": scatter_about(seeds[5], (ROWS, KV_HEADS, CACHE, HEAD_DIM), 1.0, 6.0, ((0, 8), (1, 4))),
        "lengths": draw_lengths(jax.random.fold_in(seeds[7], 71), 0),
    }


rope_base = 500000.0


def rope(values, position):
    half = values.shape[-1] // 2
    freq = rope_base ** (-2.0 * jnp.arange(half, dtype=jnp.float32) / values.shape[-1])
    angle = position.astype(jnp.float32)[:, None] * freq[None, :]
    shape = (angle.shape[0],) + (1,) * (values.ndim - 2) + (half,)
    cosine = jnp.cos(angle).reshape(shape)
    sine = jnp.sin(angle).reshape(shape)
    first = values[..., :half]
    second = values[..., half:]
    return jnp.concatenate((first * cosine - second * sine, second * cosine + first * sine), axis=-1)


def reference(hidden_in, w_query, w_keyval, w_out, key_cache, value_cache, lengths):
    w_both = jnp.concatenate((w_query, w_keyval), axis=2).reshape(D, -1)
    scale = 1.0 / (HEAD_DIM ** 0.5)
    slots = jnp.arange(CACHE, dtype=jnp.int32)
    live = slots[None, :] < lengths[:, None]
    state = hidden_in
    new_keys = []
    new_vals = []
    for step in range(STEPS):
        proj = jnp.dot(state, w_both, preferred_element_type=jnp.float32).reshape(ROWS, KV_HEADS, (GROUP + 2) * HEAD_DIM)
        position = lengths + step
        query = rope(proj[:, :, :GROUP * HEAD_DIM].reshape(ROWS, KV_HEADS, GROUP, HEAD_DIM), position).astype(jnp.bfloat16)
        new_keys.append(rope(proj[:, :, GROUP * HEAD_DIM:(GROUP + 1) * HEAD_DIM], position).astype(jnp.bfloat16))
        new_vals.append(proj[:, :, (GROUP + 1) * HEAD_DIM:].astype(jnp.bfloat16))
        keys_now = jnp.stack(new_keys, axis=2)
        vals_now = jnp.stack(new_vals, axis=2)

        def one_head(index):
            qhead = lax.dynamic_index_in_dim(query, index, 1, keepdims=False).astype(jnp.float32)
            khead = lax.dynamic_index_in_dim(key_cache, index, 1, keepdims=False).astype(jnp.float32)
            vhead = lax.dynamic_index_in_dim(value_cache, index, 1, keepdims=False).astype(jnp.float32)
            knew = lax.dynamic_index_in_dim(keys_now, index, 1, keepdims=False).astype(jnp.float32)
            vnew = lax.dynamic_index_in_dim(vals_now, index, 1, keepdims=False).astype(jnp.float32)
            cached = jnp.einsum('rjd,rcd->rjc', qhead, khead) * scale
            cached = jnp.where(live[:, None, :], cached, -1e30)
            fresh = jnp.einsum('rjd,rsd->rjs', qhead, knew) * scale
            top = jnp.maximum(jnp.max(cached, axis=-1), jnp.max(fresh, axis=-1))
            e_cached = jnp.where(live[:, None, :], jnp.exp(cached - top[..., None]), 0.0)
            e_fresh = jnp.exp(fresh - top[..., None])
            total = jnp.sum(e_cached, axis=-1) + jnp.sum(e_fresh, axis=-1)
            p_cached = (e_cached / total[..., None]).astype(jnp.bfloat16).astype(jnp.float32)
            p_fresh = (e_fresh / total[..., None]).astype(jnp.bfloat16).astype(jnp.float32)
            out = jnp.einsum('rjc,rcd->rjd', p_cached, vhead) + jnp.einsum('rjs,rsd->rjd', p_fresh, vnew)
            return out.astype(jnp.bfloat16)

        heads = lax.map(one_head, jnp.arange(KV_HEADS, dtype=jnp.int32))
        attended = jnp.transpose(heads, (1, 0, 2, 3)).reshape(ROWS, HEADS * HEAD_DIM)
        update = jnp.dot(attended, w_out, preferred_element_type=jnp.float32)
        state = (state.astype(jnp.float32) + update).astype(jnp.bfloat16)
    return state
```

```python
import jax
import jax.numpy as jnp
from jax import lax
from jax.sharding import PartitionSpec as P

STEPS = 2


rope_base = 500000.0


def rope(values, position):
    half = values.shape[-1] // 2
    freq = rope_base ** (-2.0 * jnp.arange(half, dtype=jnp.float32) / values.shape[-1])
    angle = position.astype(jnp.float32)[:, None] * freq[None, :]
    shape = (angle.shape[0],) + (1,) * (values.ndim - 2) + (half,)
    cosine = jnp.cos(angle).reshape(shape)
    sine = jnp.sin(angle).reshape(shape)
    first = values[..., :half]
    second = values[..., half:]
    return jnp.concatenate(
        (first * cosine - second * sine, second * cosine + first * sine), axis=-1
    )


def attend_step(every, step, w_q2, w_kv2, w_out, key_cache, value_cache, lengths, new_keys, new_vals):
    local_rows = key_cache.shape[0]
    groups = key_cache.shape[1]
    slots = key_cache.shape[2]
    head_dim = key_cache.shape[3]
    qcols = w_q2.shape[1]
    per_group = qcols // (groups * head_dim)
    part_q = jnp.dot(every, w_q2, preferred_element_type=jnp.float32)
    part_kv = jnp.dot(every, w_kv2, preferred_element_type=jnp.float32)
    proj = lax.psum_scatter(
        jnp.concatenate((part_q, part_kv), axis=1), "wide", scatter_dimension=0, tiled=True
    )
    position = lengths + step
    query = rope(
        proj[:, :qcols].reshape(local_rows, groups, per_group, head_dim), position
    ).astype(jnp.bfloat16)
    kv = proj[:, qcols:].reshape(local_rows, groups, 2 * head_dim)
    new_keys.append(rope(kv[:, :, :head_dim], position).astype(jnp.bfloat16))
    new_vals.append(kv[:, :, head_dim:].astype(jnp.bfloat16))
    keys_now = jnp.stack(new_keys, axis=2)
    vals_now = jnp.stack(new_vals, axis=2)
    scale = 1.0 / head_dim**0.5
    live = (jnp.arange(slots, dtype=jnp.int32)[None, :] < lengths[:, None])[:, None, None, :]
    cached = (
        jnp.einsum("rgjd,rgcd->rgjc", query, key_cache, preferred_element_type=jnp.float32) * scale
    )
    cached = jnp.where(live, cached, -1e30)
    fresh = (
        jnp.einsum("rgjd,rgsd->rgjs", query, keys_now, preferred_element_type=jnp.float32) * scale
    )
    top = jnp.maximum(jnp.max(cached, axis=-1), jnp.max(fresh, axis=-1))
    e_cached = jnp.where(live, jnp.exp(cached - top[..., None]), 0.0)
    e_fresh = jnp.exp(fresh - top[..., None])
    total = jnp.sum(e_cached, axis=-1) + jnp.sum(e_fresh, axis=-1)
    p_cached = (e_cached / total[..., None]).astype(jnp.bfloat16)
    p_fresh = (e_fresh / total[..., None]).astype(jnp.bfloat16)
    out = jnp.einsum("rgjc,rgcd->rgjd", p_cached, value_cache, preferred_element_type=jnp.float32)
    out = out + jnp.einsum("rgjs,rgsd->rgjd", p_fresh, vals_now, preferred_element_type=jnp.float32)
    attended = out.astype(jnp.bfloat16).reshape(local_rows, groups * per_group * head_dim)
    return jnp.dot(
        lax.all_gather(attended, "wide", axis=0, tiled=True),
        w_out,
        preferred_element_type=jnp.float32,
    )


def on_device(hidden_in, w_query, w_keyval, w_out, key_cache, value_cache, lengths):
    w_q2 = w_query.reshape(w_query.shape[0], -1)
    w_kv2 = w_keyval.reshape(w_keyval.shape[0], -1)
    new_keys = []
    new_vals = []
    result = hidden_in
    for step in range(STEPS):
        partial_value = attend_step(
            lax.all_gather(result, "narrow", axis=0, tiled=True),
            step,
            w_q2,
            w_kv2,
            w_out,
            key_cache,
            value_cache,
            lengths,
            new_keys,
            new_vals,
        )
        update = lax.psum_scatter(partial_value, "narrow", scatter_dimension=0, tiled=True)
        result = (result.astype(jnp.float32) + update).astype(jnp.bfloat16)
    return result


def solution(mesh):
    placed = (
        P("narrow", "wide"),
        P("wide", "narrow", None),
        P("wide", "narrow", None),
        P("narrow", "wide"),
        P("wide", "narrow", None, None),
        P("wide", "narrow", None, None),
        P("wide"),
    )
    return jax.shard_map(
        on_device, mesh=mesh, in_specs=placed, out_specs=P("narrow", "wide"), check_vma=False
    )
```

```python
import jax
import jax.numpy as jnp
from jax import lax
from jax.sharding import PartitionSpec as P

STEPS = 2
CHUNKS = 2


rope_base = 500000.0


def rope(values, position):
    half = values.shape[-1] // 2
    freq = rope_base ** (-2.0 * jnp.arange(half, dtype=jnp.float32) / values.shape[-1])
    angle = position.astype(jnp.float32)[:, None] * freq[None, :]
    shape = (angle.shape[0],) + (1,) * (values.ndim - 2) + (half,)
    cosine = jnp.cos(angle).reshape(shape)
    sine = jnp.sin(angle).reshape(shape)
    first = values[..., :half]
    second = values[..., half:]
    return jnp.concatenate(
        (first * cosine - second * sine, second * cosine + first * sine), axis=-1
    )


def attend(proj, step, key_cache, value_cache, lengths, new_keys, new_vals, qcols):
    local_rows, groups, slots, head_dim = key_cache.shape
    per_group = qcols // (groups * head_dim)
    position = lengths + step
    query = rope(
        proj[:, :qcols].reshape(local_rows, groups, per_group, head_dim), position
    ).astype(jnp.bfloat16)
    kv = proj[:, qcols:].reshape(local_rows, groups, 2 * head_dim)
    new_keys.append(rope(kv[:, :, :head_dim], position).astype(jnp.bfloat16))
    new_vals.append(kv[:, :, head_dim:].astype(jnp.bfloat16))
    keys_now = jnp.stack(new_keys, axis=2)
    vals_now = jnp.stack(new_vals, axis=2)
    scale = 1.0 / head_dim**0.5
    live = (jnp.arange(slots, dtype=jnp.int32)[None, :] < lengths[:, None])[:, None, None, :]
    cached = (
        jnp.einsum("rgjd,rgcd->rgjc", query, key_cache, preferred_element_type=jnp.float32) * scale
    )
    cached = jnp.where(live, cached, -1e30)
    fresh = (
        jnp.einsum("rgjd,rgsd->rgjs", query, keys_now, preferred_element_type=jnp.float32) * scale
    )
    top = jnp.maximum(jnp.max(cached, axis=-1), jnp.max(fresh, axis=-1))
    e_cached = jnp.where(live, jnp.exp(cached - top[..., None]), 0.0)
    e_fresh = jnp.exp(fresh - top[..., None])
    total = jnp.sum(e_cached, axis=-1) + jnp.sum(e_fresh, axis=-1)
    p_cached = (e_cached / total[..., None]).astype(jnp.bfloat16)
    p_fresh = (e_fresh / total[..., None]).astype(jnp.bfloat16)
    out = jnp.einsum("rgjc,rgcd->rgjd", p_cached, value_cache, preferred_element_type=jnp.float32)
    out = out + jnp.einsum("rgjs,rgsd->rgjd", p_fresh, vals_now, preferred_element_type=jnp.float32)
    return out.astype(jnp.bfloat16).reshape(local_rows, groups * per_group * head_dim)


def run_chunk(state, w_q2, w_kv2, w_out, key_cache, value_cache, lengths):
    qcols = w_q2.shape[1]
    new_keys = []
    new_vals = []
    for step in range(STEPS):
        every = lax.all_gather(state, "narrow", axis=0, tiled=True)
        part_q = jnp.dot(every, w_q2, preferred_element_type=jnp.float32)
        part_kv = jnp.dot(every, w_kv2, preferred_element_type=jnp.float32)
        proj = lax.psum_scatter(
            jnp.concatenate((part_q, part_kv), axis=1), "wide", scatter_dimension=0, tiled=True
        )
        attended = attend(proj, step, key_cache, value_cache, lengths, new_keys, new_vals, qcols)
        partial_value = jnp.dot(
            lax.all_gather(attended, "wide", axis=0, tiled=True),
            w_out,
            preferred_element_type=jnp.float32,
        )
        update = lax.psum_scatter(partial_value, "narrow", scatter_dimension=0, tiled=True)
        state = (state.astype(jnp.float32) + update).astype(jnp.bfloat16)
    return state


def on_device(hidden_in, w_query, w_keyval, w_out, key_cache, value_cache, lengths):
    w_q2 = w_query.reshape(w_query.shape[0], -1)
    w_kv2 = w_keyval.reshape(w_keyval.shape[0], -1)
    n_narrow = lax.axis_size("narrow")
    n_wide = lax.axis_size("wide")
    narrow_rows, cols = hidden_in.shape
    cache_rows = key_cache.shape[0]
    assert n_wide % n_narrow == 0 and cache_rows % CHUNKS == 0
    per_narrow = n_wide // n_narrow
    size = cache_rows // CHUNKS
    blocks = hidden_in.reshape(per_narrow, CHUNKS, size, cols)
    outs = []
    for c in range(CHUNKS):
        rows = slice(c * size, (c + 1) * size)
        state = blocks[:, c].reshape(per_narrow * size, cols)
        state = run_chunk(
            state, w_q2, w_kv2, w_out, key_cache[rows], value_cache[rows], lengths[rows]
        )
        outs.append(state.reshape(per_narrow, size, cols))
    return jnp.stack(outs, axis=1).reshape(narrow_rows, cols)


def solution(mesh):
    placed = (
        P("narrow", "wide"),
        P("wide", "narrow", None),
        P("wide", "narrow", None),
        P("narrow", "wide"),
        P("wide", "narrow", None, None),
        P("wide", "narrow", None, None),
        P("wide"),
    )
    return jax.shard_map(
        on_device, mesh=mesh, in_specs=placed, out_specs=P("narrow", "wide"), check_vma=False
    )
```

```python
import functools

import jax
import jax.numpy as jnp
from jax import lax
from jax.sharding import PartitionSpec as P

STEPS = 2


rope_base = 500000.0


def rope(values, position):
    half = values.shape[-1] // 2
    freq = rope_base ** (-2.0 * jnp.arange(half, dtype=jnp.float32) / values.shape[-1])
    angle = position.astype(jnp.float32)[:, None] * freq[None, :]
    shape = (angle.shape[0],) + (1,) * (values.ndim - 2) + (half,)
    cosine = jnp.cos(angle).reshape(shape)
    sine = jnp.sin(angle).reshape(shape)
    first = values[..., :half]
    second = values[..., half:]
    return jnp.concatenate(
        (first * cosine - second * sine, second * cosine + first * sine), axis=-1
    )


def line_scatter(blocks, pos, length, pairs):
    if length == 1:
        return blocks[0]
    right = None
    left = None
    for t in range(length - 1):
        b_right = jnp.clip(pos + length - 1 - t, 0, length - 1)
        b_left = jnp.clip(t + pos - length + 1, 0, length - 1)
        send_right = lax.dynamic_index_in_dim(blocks, b_right, 0, keepdims=False)
        send_left = lax.dynamic_index_in_dim(blocks, b_left, 0, keepdims=False)
        if t > 0:
            send_right = send_right + right
            send_left = send_left + left
        right = lax.ppermute(send_right, "wide", pairs(t, 1))
        left = lax.ppermute(send_left, "wide", pairs(t, -1))
    own = lax.dynamic_index_in_dim(blocks, pos, 0, keepdims=False)
    return own + right + left


def wide_scatter(value, n_x):
    n_wide = lax.axis_size("wide")
    n_z = n_wide // n_x
    w = lax.axis_index("wide")
    zpos = w // n_x
    xpos = w % n_x

    def x_pairs(t, d):
        if d > 0:
            return [(z * n_x + j, z * n_x + j + 1) for z in range(n_z) for j in range(min(t + 1, n_x - 1))]
        return [(z * n_x + j, z * n_x + j - 1) for z in range(n_z) for j in range(max(1, n_x - 1 - t), n_x)]

    def z_pairs(t, d):
        if d > 0:
            return [(j * n_x + x, (j + 1) * n_x + x) for x in range(n_x) for j in range(min(t + 1, n_z - 1))]
        return [(j * n_x + x, (j - 1) * n_x + x) for x in range(n_x) for j in range(max(1, n_z - 1 - t), n_z)]

    rows, cols = value.shape
    size = rows // n_wide
    half = cols // 2
    first = value[:, :half].reshape(n_z, n_x, size, half)
    second = value[:, half:].reshape(n_z, n_x, size, cols - half)
    a = line_scatter(jnp.swapaxes(first, 0, 1), xpos, n_x, x_pairs)
    a = line_scatter(a, zpos, n_z, z_pairs)
    b = line_scatter(second, zpos, n_z, z_pairs)
    b = line_scatter(b, xpos, n_x, x_pairs)
    return jnp.concatenate((a, b), axis=1)


def attend_step(every, step, w_q2, w_kv2, w_out, key_cache, value_cache, lengths, new_keys, new_vals, n_x):
    local_rows = key_cache.shape[0]
    groups = key_cache.shape[1]
    slots = key_cache.shape[2]
    head_dim = key_cache.shape[3]
    qcols = w_q2.shape[1]
    per_group = qcols // (groups * head_dim)
    part_q = jnp.dot(every, w_q2, preferred_element_type=jnp.float32)
    part_kv = jnp.dot(every, w_kv2, preferred_element_type=jnp.float32)
    proj = wide_scatter(jnp.concatenate((part_q, part_kv), axis=1), n_x)
    position = lengths + step
    query = rope(
        proj[:, :qcols].reshape(local_rows, groups, per_group, head_dim), position
    ).astype(jnp.bfloat16)
    kv = proj[:, qcols:].reshape(local_rows, groups, 2 * head_dim)
    new_keys.append(rope(kv[:, :, :head_dim], position).astype(jnp.bfloat16))
    new_vals.append(kv[:, :, head_dim:].astype(jnp.bfloat16))
    keys_now = jnp.stack(new_keys, axis=2)
    vals_now = jnp.stack(new_vals, axis=2)
    scale = 1.0 / head_dim**0.5
    live = (jnp.arange(slots, dtype=jnp.int32)[None, :] < lengths[:, None])[:, None, None, :]
    cached = (
        jnp.einsum("rgjd,rgcd->rgjc", query, key_cache, preferred_element_type=jnp.float32) * scale
    )
    cached = jnp.where(live, cached, -1e30)
    fresh = (
        jnp.einsum("rgjd,rgsd->rgjs", query, keys_now, preferred_element_type=jnp.float32) * scale
    )
    top = jnp.maximum(jnp.max(cached, axis=-1), jnp.max(fresh, axis=-1))
    e_cached = jnp.where(live, jnp.exp(cached - top[..., None]), 0.0)
    e_fresh = jnp.exp(fresh - top[..., None])
    total = jnp.sum(e_cached, axis=-1) + jnp.sum(e_fresh, axis=-1)
    p_cached = (e_cached / total[..., None]).astype(jnp.bfloat16)
    p_fresh = (e_fresh / total[..., None]).astype(jnp.bfloat16)
    out = jnp.einsum("rgjc,rgcd->rgjd", p_cached, value_cache, preferred_element_type=jnp.float32)
    out = out + jnp.einsum("rgjs,rgsd->rgjd", p_fresh, vals_now, preferred_element_type=jnp.float32)
    attended = out.astype(jnp.bfloat16).reshape(local_rows, groups * per_group * head_dim)
    return jnp.dot(
        lax.all_gather(attended, "wide", axis=0, tiled=True),
        w_out,
        preferred_element_type=jnp.float32,
    )


def on_device(hidden_in, w_query, w_keyval, w_out, key_cache, value_cache, lengths, n_x=1):
    w_q2 = w_query.reshape(w_query.shape[0], -1)
    w_kv2 = w_keyval.reshape(w_keyval.shape[0], -1)
    new_keys = []
    new_vals = []
    result = hidden_in
    for step in range(STEPS):
        partial_value = attend_step(
            lax.all_gather(result, "narrow", axis=0, tiled=True),
            step,
            w_q2,
            w_kv2,
            w_out,
            key_cache,
            value_cache,
            lengths,
            new_keys,
            new_vals,
            n_x,
        )
        update = lax.psum_scatter(partial_value, "narrow", scatter_dimension=0, tiled=True)
        result = (result.astype(jnp.float32) + update).astype(jnp.bfloat16)
    return result


def x_size(mesh):
    n_wide = mesh.shape["wide"]
    coords = [getattr(d, "coords", None) for d in mesh.devices.flat]
    if any(c is None for c in coords):
        return 1
    n_x = len({c[0] for c in coords})
    return n_x if n_wide % n_x == 0 else 1


def solution(mesh):
    placed = (
        P("narrow", "wide"),
        P("wide", "narrow", None),
        P("wide", "narrow", None),
        P("narrow", "wide"),
        P("wide", "narrow", None, None),
        P("wide", "narrow", None, None),
        P("wide"),
    )
    n_x = x_size(mesh)
    return jax.shard_map(
        functools.partial(on_device, n_x=n_x), mesh=mesh, in_specs=placed, out_specs=P("narrow", "wide"), check_vma=False
    )
```

```python
import jax
import jax.numpy as jnp
from jax import lax
from jax.sharding import PartitionSpec as P

STEPS = 2


rope_base = 500000.0


def rope(values, position):
    half = values.shape[-1] // 2
    freq = rope_base ** (-2.0 * jnp.arange(half, dtype=jnp.float32) / values.shape[-1])
    angle = position.astype(jnp.float32)[:, None] * freq[None, :]
    shape = (angle.shape[0],) + (1,) * (values.ndim - 2) + (half,)
    cosine = jnp.cos(angle).reshape(shape)
    sine = jnp.sin(angle).reshape(shape)
    first = values[..., :half]
    second = values[..., half:]
    return jnp.concatenate(
        (first * cosine - second * sine, second * cosine + first * sine), axis=-1
    )


def attend_step(every, step, w_q2, w_kv2, w_out, key_cache, value_cache, lengths, new_keys, new_vals):
    local_rows = key_cache.shape[0]
    groups = key_cache.shape[1]
    slots = key_cache.shape[2]
    head_dim = key_cache.shape[3]
    qcols = w_q2.shape[1]
    per_group = qcols // (groups * head_dim)
    part_q = jnp.dot(every, w_q2, preferred_element_type=jnp.float32)
    part_kv = jnp.dot(every, w_kv2, preferred_element_type=jnp.float32)
    proj = lax.psum_scatter(
        jnp.concatenate((part_q, part_kv), axis=1), "wide", scatter_dimension=0, tiled=True
    )
    position = lengths + step
    query = rope(
        proj[:, :qcols].reshape(local_rows, groups, per_group, head_dim), position
    ).astype(jnp.bfloat16)
    kv = proj[:, qcols:].reshape(local_rows, groups, 2 * head_dim)
    new_keys.append(rope(kv[:, :, :head_dim], position).astype(jnp.bfloat16))
    new_vals.append(kv[:, :, head_dim:].astype(jnp.bfloat16))
    keys_now = jnp.stack(new_keys, axis=2)
    vals_now = jnp.stack(new_vals, axis=2)
    scale = 1.0 / head_dim**0.5
    live = (jnp.arange(slots, dtype=jnp.int32)[None, :] < lengths[:, None])[:, None, None, :]
    cached = (
        jnp.einsum("rgjd,rgcd->rgjc", query, key_cache, preferred_element_type=jnp.float32) * scale
    )
    cached = jnp.where(live, cached, -1e30)
    fresh = (
        jnp.einsum("rgjd,rgsd->rgjs", query, keys_now, preferred_element_type=jnp.float32) * scale
    )
    top = jnp.maximum(jnp.max(cached, axis=-1), jnp.max(fresh, axis=-1))
    e_cached = jnp.where(live, jnp.exp(cached - top[..., None]), 0.0)
    e_fresh = jnp.exp(fresh - top[..., None])
    total = jnp.sum(e_cached, axis=-1) + jnp.sum(e_fresh, axis=-1)
    p_cached = (e_cached / total[..., None]).astype(jnp.bfloat16)
    p_fresh = (e_fresh / total[..., None]).astype(jnp.bfloat16)
    out = jnp.einsum("rgjc,rgcd->rgjd", p_cached, value_cache, preferred_element_type=jnp.float32)
    out = out + jnp.einsum("rgjs,rgsd->rgjd", p_fresh, vals_now, preferred_element_type=jnp.float32)
    attended = out.astype(jnp.bfloat16).reshape(local_rows, groups * per_group * head_dim)
    return jnp.dot(
        lax.all_gather(attended, "wide", axis=0, tiled=True),
        w_out,
        preferred_element_type=jnp.float32,
    )


def on_device(hidden_in, w_query, w_keyval, w_out, key_cache, value_cache, lengths):
    w_q2 = w_query.reshape(w_query.shape[0], -1)
    w_kv2 = w_keyval.reshape(w_keyval.shape[0], -1)
    new_keys = []
    new_vals = []
    every = lax.all_gather(hidden_in, "narrow", axis=0, tiled=True)
    for step in range(STEPS):
        partial_value = attend_step(
            every,
            step,
            w_q2,
            w_kv2,
            w_out,
            key_cache,
            value_cache,
            lengths,
            new_keys,
            new_vals,
        )
        update = lax.psum(partial_value, "narrow")
        every = (every.astype(jnp.float32) + update).astype(jnp.bfloat16)
    own = hidden_in.shape[0]
    return lax.dynamic_slice_in_dim(every, lax.axis_index("narrow") * own, own, 0)


def solution(mesh):
    placed = (
        P("narrow", "wide"),
        P("wide", "narrow", None),
        P("wide", "narrow", None),
        P("narrow", "wide"),
        P("wide", "narrow", None, None),
        P("wide", "narrow", None, None),
        P("wide"),
    )
    return jax.shard_map(
        on_device, mesh=mesh, in_specs=placed, out_specs=P("narrow", "wide"), check_vma=False
    )
```

```python
import functools

import jax
import jax.numpy as jnp
from jax import lax
from jax.sharding import PartitionSpec as P

STEPS = 2


rope_base = 500000.0


def rope(values, position):
    half = values.shape[-1] // 2
    freq = rope_base ** (-2.0 * jnp.arange(half, dtype=jnp.float32) / values.shape[-1])
    angle = position.astype(jnp.float32)[:, None] * freq[None, :]
    shape = (angle.shape[0],) + (1,) * (values.ndim - 2) + (half,)
    cosine = jnp.cos(angle).reshape(shape)
    sine = jnp.sin(angle).reshape(shape)
    first = values[..., :half]
    second = values[..., half:]
    return jnp.concatenate(
        (first * cosine - second * sine, second * cosine + first * sine), axis=-1
    )


def line_scatter(blocks, pos, length, pairs):
    if length == 1:
        return blocks[0]
    right = None
    left = None
    for t in range(length - 1):
        b_right = jnp.clip(pos + length - 1 - t, 0, length - 1)
        b_left = jnp.clip(t + pos - length + 1, 0, length - 1)
        send_right = lax.dynamic_index_in_dim(blocks, b_right, 0, keepdims=False)
        send_left = lax.dynamic_index_in_dim(blocks, b_left, 0, keepdims=False)
        if t > 0:
            send_right = send_right + right
            send_left = send_left + left
        right = lax.ppermute(send_right, "wide", pairs(t, 1))
        left = lax.ppermute(send_left, "wide", pairs(t, -1))
    own = lax.dynamic_index_in_dim(blocks, pos, 0, keepdims=False)
    return own + right + left


def wide_scatter(value, n_x):
    n_wide = lax.axis_size("wide")
    n_z = n_wide // n_x
    w = lax.axis_index("wide")
    zpos = w // n_x
    xpos = w % n_x

    def x_pairs(t, d):
        if d > 0:
            return [(z * n_x + j, z * n_x + j + 1) for z in range(n_z) for j in range(min(t + 1, n_x - 1))]
        return [(z * n_x + j, z * n_x + j - 1) for z in range(n_z) for j in range(max(1, n_x - 1 - t), n_x)]

    def z_pairs(t, d):
        if d > 0:
            return [(j * n_x + x, (j + 1) * n_x + x) for x in range(n_x) for j in range(min(t + 1, n_z - 1))]
        return [(j * n_x + x, (j - 1) * n_x + x) for x in range(n_x) for j in range(max(1, n_z - 1 - t), n_z)]

    rows, cols = value.shape
    size = rows // n_wide
    half = cols // 2
    a = lax.psum_scatter(value[:, :half], "wide", scatter_dimension=0, tiled=True)
    second = value[:, half:].reshape(n_z, n_x, size, cols - half)
    b = line_scatter(jnp.swapaxes(second, 0, 1), xpos, n_x, x_pairs)
    b = line_scatter(b, zpos, n_z, z_pairs)
    return jnp.concatenate((a, b), axis=1)


def attend_step(every, step, w_q2, w_kv2, w_out, key_cache, value_cache, lengths, new_keys, new_vals, n_x):
    local_rows = key_cache.shape[0]
    groups = key_cache.shape[1]
    slots = key_cache.shape[2]
    head_dim = key_cache.shape[3]
    qcols = w_q2.shape[1]
    per_group = qcols // (groups * head_dim)
    part_q = jnp.dot(every, w_q2, preferred_element_type=jnp.float32)
    part_kv = jnp.dot(every, w_kv2, preferred_element_type=jnp.float32)
    proj = wide_scatter(jnp.concatenate((part_q, part_kv), axis=1), n_x)
    position = lengths + step
    query = rope(
        proj[:, :qcols].reshape(local_rows, groups, per_group, head_dim), position
    ).astype(jnp.bfloat16)
    kv = proj[:, qcols:].reshape(local_rows, groups, 2 * head_dim)
    new_keys.append(rope(kv[:, :, :head_dim], position).astype(jnp.bfloat16))
    new_vals.append(kv[:, :, head_dim:].astype(jnp.bfloat16))
    keys_now = jnp.stack(new_keys, axis=2)
    vals_now = jnp.stack(new_vals, axis=2)
    scale = 1.0 / head_dim**0.5
    live = (jnp.arange(slots, dtype=jnp.int32)[None, :] < lengths[:, None])[:, None, None, :]
    cached = (
        jnp.einsum("rgjd,rgcd->rgjc", query, key_cache, preferred_element_type=jnp.float32) * scale
    )
    cached = jnp.where(live, cached, -1e30)
    fresh = (
        jnp.einsum("rgjd,rgsd->rgjs", query, keys_now, preferred_element_type=jnp.float32) * scale
    )
    top = jnp.maximum(jnp.max(cached, axis=-1), jnp.max(fresh, axis=-1))
    e_cached = jnp.where(live, jnp.exp(cached - top[..., None]), 0.0)
    e_fresh = jnp.exp(fresh - top[..., None])
    total = jnp.sum(e_cached, axis=-1) + jnp.sum(e_fresh, axis=-1)
    p_cached = (e_cached / total[..., None]).astype(jnp.bfloat16)
    p_fresh = (e_fresh / total[..., None]).astype(jnp.bfloat16)
    out = jnp.einsum("rgjc,rgcd->rgjd", p_cached, value_cache, preferred_element_type=jnp.float32)
    out = out + jnp.einsum("rgjs,rgsd->rgjd", p_fresh, vals_now, preferred_element_type=jnp.float32)
    attended = out.astype(jnp.bfloat16).reshape(local_rows, groups * per_group * head_dim)
    return jnp.dot(
        lax.all_gather(attended, "wide", axis=0, tiled=True),
        w_out,
        preferred_element_type=jnp.float32,
    )


def on_device(hidden_in, w_query, w_keyval, w_out, key_cache, value_cache, lengths, n_x=1):
    w_q2 = w_query.reshape(w_query.shape[0], -1)
    w_kv2 = w_keyval.reshape(w_keyval.shape[0], -1)
    new_keys = []
    new_vals = []
    result = hidden_in
    for step in range(STEPS):
        partial_value = attend_step(
            lax.all_gather(result, "narrow", axis=0, tiled=True),
            step,
            w_q2,
            w_kv2,
            w_out,
            key_cache,
            value_cache,
            lengths,
            new_keys,
            new_vals,
            n_x,
        )
        update = lax.psum_scatter(partial_value, "narrow", scatter_dimension=0, tiled=True)
        result = (result.astype(jnp.float32) + update).astype(jnp.bfloat16)
    return result


def x_size(mesh):
    n_wide = mesh.shape["wide"]
    coords = [getattr(d, "coords", None) for d in mesh.devices.flat]
    if any(c is None for c in coords):
        return 1
    n_x = len({c[0] for c in coords})
    return n_x if n_wide % n_x == 0 else 1


def solution(mesh):
    placed = (
        P("narrow", "wide"),
        P("wide", "narrow", None),
        P("wide", "narrow", None),
        P("narrow", "wide"),
        P("wide", "narrow", None, None),
        P("wide", "narrow", None, None),
        P("wide"),
    )
    n_x = x_size(mesh)
    return jax.shard_map(
        functools.partial(on_device, n_x=n_x), mesh=mesh, in_specs=placed, out_specs=P("narrow", "wide"), check_vma=False
    )
```

```python
import jax
import jax.numpy as jnp
from jax import lax
from jax.experimental import pallas as pl
from jax.experimental.pallas import tpu as pltpu
from jax.sharding import PartitionSpec as P

STEPS = 2


rope_base = 500000.0


def rope(values, position):
    half = values.shape[-1] // 2
    freq = rope_base ** (-2.0 * jnp.arange(half, dtype=jnp.float32) / values.shape[-1])
    angle = position.astype(jnp.float32)[:, None] * freq[None, :]
    shape = (angle.shape[0],) + (1,) * (values.ndim - 2) + (half,)
    cosine = jnp.cos(angle).reshape(shape)
    sine = jnp.sin(angle).reshape(shape)
    first = values[..., :half]
    second = values[..., half:]
    return jnp.concatenate(
        (first * cosine - second * sine, second * cosine + first * sine), axis=-1
    )


def attention_kernel(len_ref, q_ref, k_ref, v_ref, kn_ref, vn_ref, o_ref):
    groups, per_group, head_dim = q_ref.shape[1:]
    slots = k_ref.shape[2]
    fresh_count = kn_ref.shape[2]
    scale = 1.0 / head_dim**0.5
    length = len_ref[pl.program_id(0)]
    live = lax.broadcasted_iota(jnp.int32, (per_group, slots), 1) < length
    for g in range(groups):
        q = q_ref[0, g]
        cached = lax.dot_general(
            q, k_ref[0, g], (((1,), (1,)), ((), ())), preferred_element_type=jnp.float32
        ) * scale
        cached = jnp.where(live, cached, -1e30)
        qf = q.astype(jnp.float32)
        kn = kn_ref[0, g].astype(jnp.float32)
        vn = vn_ref[0, g].astype(jnp.float32)
        fresh = [
            jnp.sum(qf * kn[s : s + 1, :], axis=-1, keepdims=True) * scale
            for s in range(fresh_count)
        ]
        top = jnp.max(cached, axis=-1, keepdims=True)
        for f in fresh:
            top = jnp.maximum(top, f)
        e_cached = jnp.where(live, jnp.exp(cached - top), 0.0)
        e_fresh = [jnp.exp(f - top) for f in fresh]
        total = jnp.sum(e_cached, axis=-1, keepdims=True)
        for e in e_fresh:
            total = total + e
        p_cached = (e_cached / total).astype(jnp.bfloat16)
        out = jnp.dot(p_cached, v_ref[0, g], preferred_element_type=jnp.float32)
        fresh_out = None
        for s, e in enumerate(e_fresh):
            p = (e / total).astype(jnp.bfloat16).astype(jnp.float32)
            term = p * vn[s : s + 1, :]
            fresh_out = term if fresh_out is None else fresh_out + term
        o_ref[0, g] = (out + fresh_out).astype(o_ref.dtype)


def attention(query, key_cache, value_cache, keys_now, vals_now, lengths):
    rows, groups, per_group, head_dim = query.shape
    slots = key_cache.shape[2]
    fresh_count = keys_now.shape[2]
    row_map = lambda r, lens: (r, 0, 0, 0)
    return pl.pallas_call(
        attention_kernel,
        out_shape=jax.ShapeDtypeStruct(query.shape, jnp.bfloat16),
        grid_spec=pltpu.PrefetchScalarGridSpec(
            num_scalar_prefetch=1,
            grid=(rows,),
            in_specs=[
                pl.BlockSpec((1, groups, per_group, head_dim), row_map),
                pl.BlockSpec((1, groups, slots, head_dim), row_map),
                pl.BlockSpec((1, groups, slots, head_dim), row_map),
                pl.BlockSpec((1, groups, fresh_count, head_dim), row_map),
                pl.BlockSpec((1, groups, fresh_count, head_dim), row_map),
            ],
            out_specs=pl.BlockSpec((1, groups, per_group, head_dim), row_map),
        ),
    )(lengths, query, key_cache, value_cache, keys_now, vals_now)


def attend_step(every, step, w_q2, w_kv2, w_out, key_cache, value_cache, lengths, new_keys, new_vals):
    local_rows = key_cache.shape[0]
    groups = key_cache.shape[1]
    slots = key_cache.shape[2]
    head_dim = key_cache.shape[3]
    qcols = w_q2.shape[1]
    per_group = qcols // (groups * head_dim)
    part_q = jnp.dot(every, w_q2, preferred_element_type=jnp.float32)
    part_kv = jnp.dot(every, w_kv2, preferred_element_type=jnp.float32)
    proj = lax.psum_scatter(
        jnp.concatenate((part_q, part_kv), axis=1), "wide", scatter_dimension=0, tiled=True
    )
    position = lengths + step
    query = rope(
        proj[:, :qcols].reshape(local_rows, groups, per_group, head_dim), position
    ).astype(jnp.bfloat16)
    kv = proj[:, qcols:].reshape(local_rows, groups, 2 * head_dim)
    new_keys.append(rope(kv[:, :, :head_dim], position).astype(jnp.bfloat16))
    new_vals.append(kv[:, :, head_dim:].astype(jnp.bfloat16))
    keys_now = jnp.stack(new_keys, axis=2)
    vals_now = jnp.stack(new_vals, axis=2)
    attended = attention(query, key_cache, value_cache, keys_now, vals_now, lengths).reshape(
        local_rows, groups * per_group * head_dim
    )
    return jnp.dot(
        lax.all_gather(attended, "wide", axis=0, tiled=True),
        w_out,
        preferred_element_type=jnp.float32,
    )


def on_device(hidden_in, w_query, w_keyval, w_out, key_cache, value_cache, lengths):
    w_q2 = w_query.reshape(w_query.shape[0], -1)
    w_kv2 = w_keyval.reshape(w_keyval.shape[0], -1)
    new_keys = []
    new_vals = []
    result = hidden_in
    for step in range(STEPS):
        partial_value = attend_step(
            lax.all_gather(result, "narrow", axis=0, tiled=True),
            step,
            w_q2,
            w_kv2,
            w_out,
            key_cache,
            value_cache,
            lengths,
            new_keys,
            new_vals,
        )
        update = lax.psum_scatter(partial_value, "narrow", scatter_dimension=0, tiled=True)
        result = (result.astype(jnp.float32) + update).astype(jnp.bfloat16)
    return result


def solution(mesh):
    placed = (
        P("narrow", "wide"),
        P("wide", "narrow", None),
        P("wide", "narrow", None),
        P("narrow", "wide"),
        P("wide", "narrow", None, None),
        P("wide", "narrow", None, None),
        P("wide"),
    )
    return jax.shard_map(
        on_device, mesh=mesh, in_specs=placed, out_specs=P("narrow", "wide"), check_vma=False
    )
```

```python
import jax
import jax.numpy as jnp
from jax import lax
from jax.experimental import pallas as pl
from jax.experimental.pallas import tpu as pltpu
from jax.sharding import PartitionSpec as P

STEPS = 2


rope_base = 500000.0


def rope(values, position):
    half = values.shape[-1] // 2
    freq = rope_base ** (-2.0 * jnp.arange(half, dtype=jnp.float32) / values.shape[-1])
    angle = position.astype(jnp.float32)[:, None] * freq[None, :]
    shape = (angle.shape[0],) + (1,) * (values.ndim - 2) + (half,)
    cosine = jnp.cos(angle).reshape(shape)
    sine = jnp.sin(angle).reshape(shape)
    first = values[..., :half]
    second = values[..., half:]
    return jnp.concatenate(
        (first * cosine - second * sine, second * cosine + first * sine), axis=-1
    )


def attention_kernel(len_ref, q_ref, k_ref, v_ref, kn_ref, vn_ref, o_ref, s_ref):
    groups, per_group, head_dim = q_ref.shape[1:]
    block = s_ref.shape[2]
    fresh_count = kn_ref.shape[2]
    scale = 1.0 / head_dim**0.5
    length = len_ref[pl.program_id(0)]
    blocks = (length + block - 1) // block
    for g in range(groups):
        q = q_ref[0, g]

        def scores(b, top):
            at = pl.multiple_of(b * block, block)
            cached = lax.dot_general(
                q,
                k_ref[0, g, pl.ds(at, block), :],
                (((1,), (1,)), ((), ())),
                preferred_element_type=jnp.float32,
            ) * scale
            live = lax.broadcasted_iota(jnp.int32, (per_group, block), 1) + at < length
            cached = jnp.where(live, cached, -1e30)
            s_ref[b] = cached
            return jnp.maximum(top, jnp.max(cached, axis=-1, keepdims=True))

        top = lax.fori_loop(
            0, blocks, scores, jnp.full((per_group, 1), -jnp.inf, jnp.float32)
        )
        qf = q.astype(jnp.float32)
        kn = kn_ref[0, g].astype(jnp.float32)
        vn = vn_ref[0, g].astype(jnp.float32)
        fresh = [
            jnp.sum(qf * kn[s : s + 1, :], axis=-1, keepdims=True) * scale
            for s in range(fresh_count)
        ]
        for f in fresh:
            top = jnp.maximum(top, f)

        def exps(b, total):
            at = b * block
            live = lax.broadcasted_iota(jnp.int32, (per_group, block), 1) + at < length
            e = jnp.where(live, jnp.exp(s_ref[b] - top), 0.0)
            s_ref[b] = e
            return total + jnp.sum(e, axis=-1, keepdims=True)

        total = lax.fori_loop(0, blocks, exps, jnp.zeros((per_group, 1), jnp.float32))
        e_fresh = [jnp.exp(f - top) for f in fresh]
        for e in e_fresh:
            total = total + e

        def weighted(b, acc):
            at = pl.multiple_of(b * block, block)
            p = (s_ref[b] / total).astype(jnp.bfloat16)
            return acc + jnp.dot(
                p, v_ref[0, g, pl.ds(at, block), :], preferred_element_type=jnp.float32
            )

        out = lax.fori_loop(
            0, blocks, weighted, jnp.zeros((per_group, head_dim), jnp.float32)
        )
        for s, e in enumerate(e_fresh):
            p = (e / total).astype(jnp.bfloat16).astype(jnp.float32)
            out = out + p * vn[s : s + 1, :]
        o_ref[0, g] = out.astype(o_ref.dtype)


SLOT_BLOCK = 256


def attention(query, key_cache, value_cache, keys_now, vals_now, lengths):
    rows, groups, per_group, head_dim = query.shape
    slots = key_cache.shape[2]
    fresh_count = keys_now.shape[2]
    row_map = lambda r, lens: (r, 0, 0, 0)
    return pl.pallas_call(
        attention_kernel,
        out_shape=jax.ShapeDtypeStruct(query.shape, jnp.bfloat16),
        grid_spec=pltpu.PrefetchScalarGridSpec(
            num_scalar_prefetch=1,
            grid=(rows,),
            in_specs=[
                pl.BlockSpec((1, groups, per_group, head_dim), row_map),
                pl.BlockSpec((1, groups, slots, head_dim), row_map),
                pl.BlockSpec((1, groups, slots, head_dim), row_map),
                pl.BlockSpec((1, groups, fresh_count, head_dim), row_map),
                pl.BlockSpec((1, groups, fresh_count, head_dim), row_map),
            ],
            out_specs=pl.BlockSpec((1, groups, per_group, head_dim), row_map),
            scratch_shapes=[
                pltpu.VMEM((slots // SLOT_BLOCK, per_group, SLOT_BLOCK), jnp.float32)
            ],
        ),
    )(lengths, query, key_cache, value_cache, keys_now, vals_now)


def attend_step(every, step, w_q2, w_kv2, w_out, key_cache, value_cache, lengths, new_keys, new_vals):
    local_rows = key_cache.shape[0]
    groups = key_cache.shape[1]
    slots = key_cache.shape[2]
    head_dim = key_cache.shape[3]
    qcols = w_q2.shape[1]
    per_group = qcols // (groups * head_dim)
    part_q = jnp.dot(every, w_q2, preferred_element_type=jnp.float32)
    part_kv = jnp.dot(every, w_kv2, preferred_element_type=jnp.float32)
    proj = lax.psum_scatter(
        jnp.concatenate((part_q, part_kv), axis=1), "wide", scatter_dimension=0, tiled=True
    )
    position = lengths + step
    query = rope(
        proj[:, :qcols].reshape(local_rows, groups, per_group, head_dim), position
    ).astype(jnp.bfloat16)
    kv = proj[:, qcols:].reshape(local_rows, groups, 2 * head_dim)
    new_keys.append(rope(kv[:, :, :head_dim], position).astype(jnp.bfloat16))
    new_vals.append(kv[:, :, head_dim:].astype(jnp.bfloat16))
    keys_now = jnp.stack(new_keys, axis=2)
    vals_now = jnp.stack(new_vals, axis=2)
    attended = attention(query, key_cache, value_cache, keys_now, vals_now, lengths).reshape(
        local_rows, groups * per_group * head_dim
    )
    return jnp.dot(
        lax.all_gather(attended, "wide", axis=0, tiled=True),
        w_out,
        preferred_element_type=jnp.float32,
    )


def on_device(hidden_in, w_query, w_keyval, w_out, key_cache, value_cache, lengths):
    w_q2 = w_query.reshape(w_query.shape[0], -1)
    w_kv2 = w_keyval.reshape(w_keyval.shape[0], -1)
    new_keys = []
    new_vals = []
    result = hidden_in
    for step in range(STEPS):
        partial_value = attend_step(
            lax.all_gather(result, "narrow", axis=0, tiled=True),
            step,
            w_q2,
            w_kv2,
            w_out,
            key_cache,
            value_cache,
            lengths,
            new_keys,
            new_vals,
        )
        update = lax.psum_scatter(partial_value, "narrow", scatter_dimension=0, tiled=True)
        result = (result.astype(jnp.float32) + update).astype(jnp.bfloat16)
    return result


def solution(mesh):
    placed = (
        P("narrow", "wide"),
        P("wide", "narrow", None),
        P("wide", "narrow", None),
        P("narrow", "wide"),
        P("wide", "narrow", None, None),
        P("wide", "narrow", None, None),
        P("wide"),
    )
    return jax.shard_map(
        on_device, mesh=mesh, in_specs=placed, out_specs=P("narrow", "wide"), check_vma=False
    )
```

```python
import jax
import jax.numpy as jnp
from jax import lax
from jax.sharding import PartitionSpec as P

STEPS = 2


rope_base = 500000.0


def rope(values, position):
    half = values.shape[-1] // 2
    freq = rope_base ** (-2.0 * jnp.arange(half, dtype=jnp.float32) / values.shape[-1])
    angle = position.astype(jnp.float32)[:, None] * freq[None, :]
    shape = (angle.shape[0],) + (1,) * (values.ndim - 2) + (half,)
    cosine = jnp.cos(angle).reshape(shape)
    sine = jnp.sin(angle).reshape(shape)
    first = values[..., :half]
    second = values[..., half:]
    return jnp.concatenate(
        (first * cosine - second * sine, second * cosine + first * sine), axis=-1
    )


def attend_step(every, step, w_q2, w_kv2, w_out, key_cache, value_cache, lengths, new_keys, new_vals):
    local_rows = key_cache.shape[0]
    groups = key_cache.shape[1]
    slots = key_cache.shape[2]
    head_dim = key_cache.shape[3]
    qcols = w_q2.shape[1]
    per_group = qcols // (groups * head_dim)
    part_q = jnp.dot(every, w_q2, preferred_element_type=jnp.float32)
    part_kv = jnp.dot(every, w_kv2, preferred_element_type=jnp.float32)
    proj = lax.psum_scatter(
        jnp.concatenate((part_q, part_kv), axis=1), "wide", scatter_dimension=0, tiled=True
    )
    position = lengths + step
    query = rope(
        proj[:, :qcols].reshape(local_rows, groups, per_group, head_dim), position
    ).astype(jnp.bfloat16)
    kv = proj[:, qcols:].reshape(local_rows, groups, 2 * head_dim)
    new_keys.append(rope(kv[:, :, :head_dim], position).astype(jnp.bfloat16))
    new_vals.append(kv[:, :, head_dim:].astype(jnp.bfloat16))
    keys_now = jnp.stack(new_keys, axis=2)
    vals_now = jnp.stack(new_vals, axis=2)
    scale = 1.0 / head_dim**0.5
    live = (jnp.arange(slots, dtype=jnp.int32)[None, :] < lengths[:, None])[:, None, :]
    width = per_group * head_dim
    total_update = None
    for g in range(groups):
        q = query[:, g]
        cached = (
            jnp.einsum("rjd,rcd->rjc", q, key_cache[:, g], preferred_element_type=jnp.float32)
            * scale
        )
        cached = jnp.where(live, cached, -1e30)
        fresh = (
            jnp.einsum("rjd,rsd->rjs", q, keys_now[:, g], preferred_element_type=jnp.float32)
            * scale
        )
        top = jnp.maximum(jnp.max(cached, axis=-1), jnp.max(fresh, axis=-1))
        e_cached = jnp.where(live, jnp.exp(cached - top[..., None]), 0.0)
        e_fresh = jnp.exp(fresh - top[..., None])
        total = jnp.sum(e_cached, axis=-1) + jnp.sum(e_fresh, axis=-1)
        p_cached = (e_cached / total[..., None]).astype(jnp.bfloat16)
        p_fresh = (e_fresh / total[..., None]).astype(jnp.bfloat16)
        out = jnp.einsum(
            "rjc,rcd->rjd", p_cached, value_cache[:, g], preferred_element_type=jnp.float32
        )
        out = out + jnp.einsum(
            "rjs,rsd->rjd", p_fresh, vals_now[:, g], preferred_element_type=jnp.float32
        )
        attended = out.astype(jnp.bfloat16).reshape(local_rows, width)
        update = jnp.dot(
            lax.all_gather(attended, "wide", axis=0, tiled=True),
            w_out[g * width : (g + 1) * width],
            preferred_element_type=jnp.float32,
        )
        total_update = update if total_update is None else total_update + update
    return total_update


def on_device(hidden_in, w_query, w_keyval, w_out, key_cache, value_cache, lengths):
    w_q2 = w_query.reshape(w_query.shape[0], -1)
    w_kv2 = w_keyval.reshape(w_keyval.shape[0], -1)
    new_keys = []
    new_vals = []
    result = hidden_in
    for step in range(STEPS):
        partial_value = attend_step(
            lax.all_gather(result, "narrow", axis=0, tiled=True),
            step,
            w_q2,
            w_kv2,
            w_out,
            key_cache,
            value_cache,
            lengths,
            new_keys,
            new_vals,
        )
        update = lax.psum_scatter(partial_value, "narrow", scatter_dimension=0, tiled=True)
        result = (result.astype(jnp.float32) + update).astype(jnp.bfloat16)
    return result


def solution(mesh):
    placed = (
        P("narrow", "wide"),
        P("wide", "narrow", None),
        P("wide", "narrow", None),
        P("narrow", "wide"),
        P("wide", "narrow", None, None),
        P("wide", "narrow", None, None),
        P("wide"),
    )
    return jax.shard_map(
        on_device, mesh=mesh, in_specs=placed, out_specs=P("narrow", "wide"), check_vma=False
    )
```

```python
import jax
import jax.numpy as jnp
from jax import lax
from jax.sharding import PartitionSpec as P

STEPS = 2


rope_base = 500000.0


def rope(values, position):
    half = values.shape[-1] // 2
    freq = rope_base ** (-2.0 * jnp.arange(half, dtype=jnp.float32) / values.shape[-1])
    angle = position.astype(jnp.float32)[:, None] * freq[None, :]
    shape = (angle.shape[0],) + (1,) * (values.ndim - 2) + (half,)
    cosine = jnp.cos(angle).reshape(shape)
    sine = jnp.sin(angle).reshape(shape)
    first = values[..., :half]
    second = values[..., half:]
    return jnp.concatenate(
        (first * cosine - second * sine, second * cosine + first * sine), axis=-1
    )


def attend_step(every, step, w_q2, w_kv2, w_out, key_cache, value_cache, lengths, new_keys, new_vals):
    local_rows = key_cache.shape[0]
    groups = key_cache.shape[1]
    slots = key_cache.shape[2]
    head_dim = key_cache.shape[3]
    qcols = w_q2.shape[1]
    per_group = qcols // (groups * head_dim)
    part_q = jnp.dot(every, w_q2, preferred_element_type=jnp.float32)
    part_kv = jnp.dot(every, w_kv2, preferred_element_type=jnp.float32)
    proj = lax.psum_scatter(
        jnp.concatenate((part_q, part_kv), axis=1), "wide", scatter_dimension=0, tiled=True
    )
    position = lengths + step
    query = rope(
        proj[:, :qcols].reshape(local_rows, groups, per_group, head_dim), position
    ).astype(jnp.bfloat16)
    kv = proj[:, qcols:].reshape(local_rows, groups, 2 * head_dim)
    new_keys.append(rope(kv[:, :, :head_dim], position).astype(jnp.bfloat16))
    new_vals.append(kv[:, :, head_dim:].astype(jnp.bfloat16))
    keys_now = jnp.stack(new_keys, axis=2)
    vals_now = jnp.stack(new_vals, axis=2)
    scale = 1.0 / head_dim**0.5
    live = (jnp.arange(slots, dtype=jnp.int32)[None, :] < lengths[:, None])[:, None, None, :]
    cached = (
        jnp.einsum("rgjd,rgcd->rgjc", query, key_cache, preferred_element_type=jnp.float32) * scale
    )
    cached = jnp.where(live, cached, -1e30)
    fresh = (
        jnp.einsum("rgjd,rgsd->rgjs", query, keys_now, preferred_element_type=jnp.float32) * scale
    )
    top = jnp.maximum(jnp.max(cached, axis=-1), jnp.max(fresh, axis=-1))
    e_cached = jnp.where(live, jnp.exp(cached - top[..., None]), 0.0)
    e_fresh = jnp.exp(fresh - top[..., None])
    total = jnp.sum(e_cached, axis=-1) + jnp.sum(e_fresh, axis=-1)
    p_cached = (e_cached / total[..., None]).astype(jnp.bfloat16)
    p_fresh = (e_fresh / total[..., None]).astype(jnp.bfloat16)
    out = jnp.einsum("rgjc,rgcd->rgjd", p_cached, value_cache, preferred_element_type=jnp.float32)
    out = out + jnp.einsum("rgjs,rgsd->rgjd", p_fresh, vals_now, preferred_element_type=jnp.float32)
    attended = out.astype(jnp.bfloat16).reshape(local_rows, groups * per_group * head_dim)
    return jnp.dot(
        lax.all_gather(attended, "wide", axis=0, tiled=True),
        w_out,
        preferred_element_type=jnp.float32,
    )


def narrow_gather(state, n_narrow):
    rows, cols = state.shape
    half = rows // 2
    parts = [
        lax.all_gather(state[h * half : (h + 1) * half], "narrow", axis=0, tiled=True).reshape(
            n_narrow, 1, half, cols
        )
        for h in range(2)
    ]
    return jnp.concatenate(parts, axis=1).reshape(n_narrow * rows, cols)


def narrow_scatter(value, n_narrow):
    rows, cols = value.shape
    half = rows // n_narrow // 2
    blocks = value.reshape(n_narrow, 2, half, cols)
    parts = [
        lax.psum_scatter(
            blocks[:, h].reshape(n_narrow * half, cols), "narrow", scatter_dimension=0, tiled=True
        )
        for h in range(2)
    ]
    return jnp.concatenate(parts, axis=0)


def on_device(hidden_in, w_query, w_keyval, w_out, key_cache, value_cache, lengths):
    w_q2 = w_query.reshape(w_query.shape[0], -1)
    w_kv2 = w_keyval.reshape(w_keyval.shape[0], -1)
    n_narrow = lax.axis_size("narrow")
    new_keys = []
    new_vals = []
    result = hidden_in
    for step in range(STEPS):
        partial_value = attend_step(
            narrow_gather(result, n_narrow),
            step,
            w_q2,
            w_kv2,
            w_out,
            key_cache,
            value_cache,
            lengths,
            new_keys,
            new_vals,
        )
        update = narrow_scatter(partial_value, n_narrow)
        result = (result.astype(jnp.float32) + update).astype(jnp.bfloat16)
    return result


def solution(mesh):
    placed = (
        P("narrow", "wide"),
        P("wide", "narrow", None),
        P("wide", "narrow", None),
        P("narrow", "wide"),
        P("wide", "narrow", None, None),
        P("wide", "narrow", None, None),
        P("wide"),
    )
    return jax.shard_map(
        on_device, mesh=mesh, in_specs=placed, out_specs=P("narrow", "wide"), check_vma=False
    )
```

```python
import jax
import jax.numpy as jnp
from jax import lax
from jax.sharding import PartitionSpec as P

STEPS = 2


rope_base = 500000.0


def rope(values, position):
    half = values.shape[-1] // 2
    freq = rope_base ** (-2.0 * jnp.arange(half, dtype=jnp.float32) / values.shape[-1])
    angle = position.astype(jnp.float32)[:, None] * freq[None, :]
    shape = (angle.shape[0],) + (1,) * (values.ndim - 2) + (half,)
    cosine = jnp.cos(angle).reshape(shape)
    sine = jnp.sin(angle).reshape(shape)
    first = values[..., :half]
    second = values[..., half:]
    return jnp.concatenate(
        (first * cosine - second * sine, second * cosine + first * sine), axis=-1
    )


def attend_step(every, step, w_q2, w_kv2, w_out, key_cache, value_cache, lengths, new_keys, new_vals):
    local_rows = key_cache.shape[0]
    groups = key_cache.shape[1]
    slots = key_cache.shape[2]
    head_dim = key_cache.shape[3]
    qcols = w_q2.shape[1]
    per_group = qcols // (groups * head_dim)
    part_q = jnp.dot(every, w_q2, preferred_element_type=jnp.float32)
    part_kv = jnp.dot(every, w_kv2, preferred_element_type=jnp.float32)
    proj = lax.psum_scatter(
        jnp.concatenate((part_q, part_kv), axis=1), "wide", scatter_dimension=0, tiled=True
    )
    position = lengths + step
    query = rope(
        proj[:, :qcols].reshape(local_rows, groups, per_group, head_dim), position
    ).astype(jnp.bfloat16)
    kv = proj[:, qcols:].reshape(local_rows, groups, 2 * head_dim)
    new_keys.append(rope(kv[:, :, :head_dim], position).astype(jnp.bfloat16))
    new_vals.append(kv[:, :, head_dim:].astype(jnp.bfloat16))
    keys_now = jnp.stack(new_keys, axis=2)
    vals_now = jnp.stack(new_vals, axis=2)
    scale = 1.0 / head_dim**0.5
    live = (jnp.arange(slots, dtype=jnp.int32)[None, :] < lengths[:, None])[:, None, None, :]
    cached = (
        jnp.einsum("rgjd,rgcd->rgjc", query, key_cache, preferred_element_type=jnp.float32) * scale
    )
    cached = jnp.where(live, cached, -1e30)
    fresh = (
        jnp.einsum("rgjd,rgsd->rgjs", query, keys_now, preferred_element_type=jnp.float32) * scale
    )
    top = jnp.maximum(jnp.max(cached, axis=-1), jnp.max(fresh, axis=-1))
    e_cached = jnp.where(live, jnp.exp(cached - top[..., None]), 0.0)
    e_fresh = jnp.exp(fresh - top[..., None])
    total = jnp.sum(e_cached, axis=-1) + jnp.sum(e_fresh, axis=-1)
    p_cached = (e_cached / total[..., None]).astype(jnp.bfloat16)
    p_fresh = (e_fresh / total[..., None]).astype(jnp.bfloat16)
    out = jnp.einsum("rgjc,rgcd->rgjd", p_cached, value_cache, preferred_element_type=jnp.float32)
    out = out + jnp.einsum("rgjs,rgsd->rgjd", p_fresh, vals_now, preferred_element_type=jnp.float32)
    attended = out.astype(jnp.bfloat16).reshape(local_rows, groups * per_group * head_dim)
    return jnp.dot(
        lax.all_gather(attended, "wide", axis=0, tiled=True),
        w_out,
        preferred_element_type=jnp.float32,
    )


def narrow_gather(state, n_narrow):
    rows, cols = state.shape
    half = rows // 2
    parts = [
        lax.all_gather(state[h * half : (h + 1) * half], "narrow", axis=0, tiled=True).reshape(
            n_narrow, 1, half, cols
        )
        for h in range(2)
    ]
    return jnp.concatenate(parts, axis=1).reshape(n_narrow * rows, cols)


def on_device(hidden_in, w_query, w_keyval, w_out, key_cache, value_cache, lengths):
    w_q2 = w_query.reshape(w_query.shape[0], -1)
    w_kv2 = w_keyval.reshape(w_keyval.shape[0], -1)
    new_keys = []
    new_vals = []
    result = hidden_in
    for step in range(STEPS):
        partial_value = attend_step(
            lax.all_gather(result, "narrow", axis=0, tiled=True)
            if step == 0
            else narrow_gather(result, lax.axis_size("narrow")),
            step,
            w_q2,
            w_kv2,
            w_out,
            key_cache,
            value_cache,
            lengths,
            new_keys,
            new_vals,
        )
        update = lax.psum_scatter(partial_value, "narrow", scatter_dimension=0, tiled=True)
        result = (result.astype(jnp.float32) + update).astype(jnp.bfloat16)
    return result


def solution(mesh):
    placed = (
        P("narrow", "wide"),
        P("wide", "narrow", None),
        P("wide", "narrow", None),
        P("narrow", "wide"),
        P("wide", "narrow", None, None),
        P("wide", "narrow", None, None),
        P("wide"),
    )
    return jax.shard_map(
        on_device, mesh=mesh, in_specs=placed, out_specs=P("narrow", "wide"), check_vma=False
    )
```

```python
import jax
import jax.numpy as jnp
from jax import lax
from jax.sharding import PartitionSpec as P

STEPS = 2


rope_base = 500000.0


def rope(values, position):
    half = values.shape[-1] // 2
    freq = rope_base ** (-2.0 * jnp.arange(half, dtype=jnp.float32) / values.shape[-1])
    angle = position.astype(jnp.float32)[:, None] * freq[None, :]
    shape = (angle.shape[0],) + (1,) * (values.ndim - 2) + (half,)
    cosine = jnp.cos(angle).reshape(shape)
    sine = jnp.sin(angle).reshape(shape)
    first = values[..., :half]
    second = values[..., half:]
    return jnp.concatenate(
        (first * cosine - second * sine, second * cosine + first * sine), axis=-1
    )


def attend_step(every, step, w_q2, w_kv2, w_out, key_cache, value_cache, lengths, new_keys, new_vals):
    local_rows = key_cache.shape[0]
    groups = key_cache.shape[1]
    slots = key_cache.shape[2]
    head_dim = key_cache.shape[3]
    qcols = w_q2.shape[1]
    per_group = qcols // (groups * head_dim)
    part_q = jnp.dot(every, w_q2, preferred_element_type=jnp.float32)
    part_kv = jnp.dot(every, w_kv2, preferred_element_type=jnp.float32)
    proj = lax.psum_scatter(
        jnp.concatenate((part_q, part_kv), axis=1), "wide", scatter_dimension=0, tiled=True
    )
    position = lengths + step
    query = rope(
        proj[:, :qcols].reshape(local_rows, groups, per_group, head_dim), position
    ).astype(jnp.bfloat16)
    kv = proj[:, qcols:].reshape(local_rows, groups, 2 * head_dim)
    new_keys.append(rope(kv[:, :, :head_dim], position).astype(jnp.bfloat16))
    new_vals.append(kv[:, :, head_dim:].astype(jnp.bfloat16))
    keys_now = jnp.stack(new_keys, axis=2)
    vals_now = jnp.stack(new_vals, axis=2)
    scale = 1.0 / head_dim**0.5
    live = (jnp.arange(slots, dtype=jnp.int32)[None, :] < lengths[:, None])[:, None, None, :]
    cached = (
        jnp.einsum("rgjd,rgcd->rgjc", query, key_cache, preferred_element_type=jnp.float32) * scale
    )
    cached = jnp.where(live, cached, -1e30)
    fresh = (
        jnp.einsum("rgjd,rgsd->rgjs", query, keys_now, preferred_element_type=jnp.float32) * scale
    )
    top = jnp.maximum(jnp.max(cached, axis=-1), jnp.max(fresh, axis=-1))
    e_cached = jnp.where(live, jnp.exp(cached - top[..., None]), 0.0)
    e_fresh = jnp.exp(fresh - top[..., None])
    total = jnp.sum(e_cached, axis=-1) + jnp.sum(e_fresh, axis=-1)
    p_cached = (e_cached / total[..., None]).astype(jnp.bfloat16)
    p_fresh = (e_fresh / total[..., None]).astype(jnp.bfloat16)
    out = jnp.einsum("rgjc,rgcd->rgjd", p_cached, value_cache, preferred_element_type=jnp.float32)
    out = out + jnp.einsum("rgjs,rgsd->rgjd", p_fresh, vals_now, preferred_element_type=jnp.float32)
    attended = out.astype(jnp.bfloat16).reshape(local_rows, groups * per_group * head_dim)
    return jnp.dot(
        jnp.concatenate(
            [
                lax.all_gather(attended[:, i * 1024 : (i + 1) * 1024], "wide", axis=0, tiled=True)
                for i in range(attended.shape[1] // 1024)
            ],
            axis=1,
        ),
        w_out,
        preferred_element_type=jnp.float32,
    )


def narrow_gather(state, n_narrow):
    rows, cols = state.shape
    half = rows // 2
    parts = [
        lax.all_gather(state[h * half : (h + 1) * half], "narrow", axis=0, tiled=True).reshape(
            n_narrow, 1, half, cols
        )
        for h in range(2)
    ]
    return jnp.concatenate(parts, axis=1).reshape(n_narrow * rows, cols)


def on_device(hidden_in, w_query, w_keyval, w_out, key_cache, value_cache, lengths):
    w_q2 = w_query.reshape(w_query.shape[0], -1)
    w_kv2 = w_keyval.reshape(w_keyval.shape[0], -1)
    new_keys = []
    new_vals = []
    result = hidden_in
    for step in range(STEPS):
        partial_value = attend_step(
            lax.all_gather(result, "narrow", axis=0, tiled=True)
            if step == 0
            else narrow_gather(result, lax.axis_size("narrow")),
            step,
            w_q2,
            w_kv2,
            w_out,
            key_cache,
            value_cache,
            lengths,
            new_keys,
            new_vals,
        )
        update = lax.psum_scatter(partial_value, "narrow", scatter_dimension=0, tiled=True)
        result = (result.astype(jnp.float32) + update).astype(jnp.bfloat16)
    return result


def solution(mesh):
    placed = (
        P("narrow", "wide"),
        P("wide", "narrow", None),
        P("wide", "narrow", None),
        P("narrow", "wide"),
        P("wide", "narrow", None, None),
        P("wide", "narrow", None, None),
        P("wide"),
    )
    return jax.shard_map(
        on_device, mesh=mesh, in_specs=placed, out_specs=P("narrow", "wide"), check_vma=False
    )
```

```python
import jax
import jax.numpy as jnp
from jax import lax
from jax.sharding import PartitionSpec as P

STEPS = 2


rope_base = 500000.0


def rope(values, position):
    half = values.shape[-1] // 2
    freq = rope_base ** (-2.0 * jnp.arange(half, dtype=jnp.float32) / values.shape[-1])
    angle = position.astype(jnp.float32)[:, None] * freq[None, :]
    shape = (angle.shape[0],) + (1,) * (values.ndim - 2) + (half,)
    cosine = jnp.cos(angle).reshape(shape)
    sine = jnp.sin(angle).reshape(shape)
    first = values[..., :half]
    second = values[..., half:]
    return jnp.concatenate(
        (first * cosine - second * sine, second * cosine + first * sine), axis=-1
    )


def attend_step(every, step, w_q2, w_kv2, w_out, key_cache, value_cache, lengths, new_keys, new_vals):
    local_rows = key_cache.shape[0]
    groups = key_cache.shape[1]
    slots = key_cache.shape[2]
    head_dim = key_cache.shape[3]
    qcols = w_q2.shape[1]
    per_group = qcols // (groups * head_dim)
    part_q = jnp.dot(every, w_q2, preferred_element_type=jnp.float32)
    part_kv = jnp.dot(every, w_kv2, preferred_element_type=jnp.float32)
    proj = lax.psum_scatter(
        jnp.concatenate((part_q, part_kv), axis=1), "wide", scatter_dimension=0, tiled=True
    )
    position = lengths + step
    query = rope(
        proj[:, :qcols].reshape(local_rows, groups, per_group, head_dim), position
    ).astype(jnp.bfloat16)
    kv = proj[:, qcols:].reshape(local_rows, groups, 2 * head_dim)
    new_keys.append(rope(kv[:, :, :head_dim], position).astype(jnp.bfloat16))
    new_vals.append(kv[:, :, head_dim:].astype(jnp.bfloat16))
    keys_now = jnp.stack(new_keys, axis=2)
    vals_now = jnp.stack(new_vals, axis=2)
    scale = 1.0 / head_dim**0.5
    live = (jnp.arange(slots, dtype=jnp.int32)[None, :] < lengths[:, None])[:, None, None, :]
    cached = (
        jnp.einsum("rgjd,rgcd->rgjc", query, key_cache, preferred_element_type=jnp.float32) * scale
    )
    cached = jnp.where(live, cached, -1e30)
    fresh = (
        jnp.einsum("rgjd,rgsd->rgjs", query, keys_now, preferred_element_type=jnp.float32) * scale
    )
    top = jnp.maximum(jnp.max(cached, axis=-1), jnp.max(fresh, axis=-1))
    e_cached = jnp.where(live, jnp.exp(cached - top[..., None]), 0.0)
    e_fresh = jnp.exp(fresh - top[..., None])
    total = jnp.sum(e_cached, axis=-1) + jnp.sum(e_fresh, axis=-1)
    p_cached = (e_cached / total[..., None]).astype(jnp.bfloat16)
    p_fresh = (e_fresh / total[..., None]).astype(jnp.bfloat16)
    out = jnp.einsum("rgjc,rgcd->rgjd", p_cached, value_cache, preferred_element_type=jnp.float32)
    out = out + jnp.einsum("rgjs,rgsd->rgjd", p_fresh, vals_now, preferred_element_type=jnp.float32)
    attended = out.astype(jnp.bfloat16).reshape(local_rows, groups * per_group * head_dim)
    return jnp.dot(
        lax.all_gather(attended, "wide", axis=0, tiled=True),
        w_out,
        preferred_element_type=jnp.float32,
    )


def narrow_gather(state, n_narrow):
    rows, cols = state.shape
    pieces = 4
    half = rows // pieces
    parts = [
        lax.all_gather(state[h * half : (h + 1) * half], "narrow", axis=0, tiled=True).reshape(
            n_narrow, 1, half, cols
        )
        for h in range(pieces)
    ]
    return jnp.concatenate(parts, axis=1).reshape(n_narrow * rows, cols)


def on_device(hidden_in, w_query, w_keyval, w_out, key_cache, value_cache, lengths):
    w_q2 = w_query.reshape(w_query.shape[0], -1)
    w_kv2 = w_keyval.reshape(w_keyval.shape[0], -1)
    new_keys = []
    new_vals = []
    result = hidden_in
    for step in range(STEPS):
        partial_value = attend_step(
            lax.all_gather(result, "narrow", axis=0, tiled=True)
            if step == 0
            else narrow_gather(result, lax.axis_size("narrow")),
            step,
            w_q2,
            w_kv2,
            w_out,
            key_cache,
            value_cache,
            lengths,
            new_keys,
            new_vals,
        )
        update = lax.psum_scatter(partial_value, "narrow", scatter_dimension=0, tiled=True)
        result = (result.astype(jnp.float32) + update).astype(jnp.bfloat16)
    return result


def solution(mesh):
    placed = (
        P("narrow", "wide"),
        P("wide", "narrow", None),
        P("wide", "narrow", None),
        P("narrow", "wide"),
        P("wide", "narrow", None, None),
        P("wide", "narrow", None, None),
        P("wide"),
    )
    return jax.shard_map(
        on_device, mesh=mesh, in_specs=placed, out_specs=P("narrow", "wide"), check_vma=False
    )
```
